256 devices in a mesh: aux: 16 (over z_hi, y, core), virt: 16 (over x, z_lo).
Axes of the slice: x: 4, y: 4, z: 8 (z_hi: 2, z_lo: 4; z = z_hi * 4 + z_lo), core: 2. Of those that a mesh axis runs over, the one named last changes fastest.
Arguments:
- row_codes: bfloat16 [16, 128, 1920], P('aux'), may hold values from -4 to 4
- row_scales: float32 [16, 128, 15], P('aux'), may hold values from 0.2 to 2
- panel_codes: bfloat16 [16, 1920, 1920], P('aux', 'virt'), may hold values from -4 to 4
- panel_scales: float32 [16, 1920, 15], P('aux', 'virt'), may hold values from 0.0017116329 to 0.01711633
- amplitudes: bfloat16 [64, 1920, 1920], P('aux', 'virt'), may hold values from -0.125 to 0.125
Outputs:
- residual: float32 [1920, 64, 128], P('virt', 'aux')
The draws below stay inside these ranges and needn't reach their ends.
All inputs are finite; a program needn't handle non-finite values.
Results may differ from the reference program's by a relative error of at most 0.005.
Values may be sent and summed in bfloat16 or wider, within the bound.
No kernel may reach another device: no remote copies, remote signals or barrier semaphores. Data moves between devices by JAX's collectives and lax.ppermute only.
A program may use at most 128 MiB of HBM per device.

```python
import math
import jax
import jax.numpy as jnp
from jax import lax

V = 1920
BLK = 128
AW = 128
NQ = 16
NPAIRS = 64
NBLK = 15


def spiked(values, key, source, target, blocks, factor):
    owner, partner = [(jnp.arange(values.shape[axis_at]) // (values.shape[axis_at] // blocks)).reshape([-1 if axis == axis_at else 1 for axis in range(values.ndim)]) for axis_at in (source, target)]
    chosen = jax.random.permutation(key, blocks)[partner]
    strong = (owner == chosen) | (owner == (partner + blocks // 2) % blocks)
    return jnp.where(strong, factor * values, values)


def levels(rng, shape, split, low, high):
    def one(dim, shards_of):
        draws = jax.random.uniform(jax.random.fold_in(jax.random.fold_in(rng, 6), dim), (shards_of,), jnp.float32, low / len(split), high / len(split))
        return jnp.repeat(jnp.exp(draws), shape[dim] // shards_of).reshape((-1,) + (1,) * (len(shape) - dim - 1))

    factor_of = one(*split[0])
    for cut in split[1:]:
        factor_of = factor_of * one(*cut)
    return factor_of


def scatter_about(key, shape, spread, reach, cuts=(), held_as=jnp.bfloat16):
    drawn = jax.random.normal(key, shape, jnp.float32) * spread
    if len(cuts) > 0:
        drawn = levels(key, shape, cuts, -0.22, 0.18) * drawn
    return jnp.clip(drawn, min=-reach, max=reach).astype(held_as)


def noise_with(own_key, extent, spread, most, pieces, heavy, kind=jnp.bfloat16):
    drawn = spread * jax.random.normal(own_key, extent, jnp.float32)
    if pieces:
        drawn = drawn * levels(own_key, extent, pieces, -0.22, 0.18)
    return jnp.clip(spiked(drawn, jax.random.fold_in(own_key, 3), *heavy), -most, most).astype(kind)


def setup_inputs(seed: int = 0) -> dict:
    key_list = jax.random.split(jax.random.key(seed), 6)
    return {
        "row_codes": scatter_about(key_list[0], (NQ, AW, V), 1.0, 4.0, ((0, 16),)),
        "row_scales": jnp.clip(jnp.exp(math.log(2.0) - 2.3025851 * jax.random.uniform(key_list[1], (NQ, AW, NBLK), jnp.float32) ** levels(key_list[1], (NQ, AW, NBLK), ((0, 16),), -0.2, 0.2)), 0.2, 2.0),
        "panel_codes": noise_with(key_list[2], (NQ, V, V), 1.0, 4.0, ((0, 16), (1, 16)), (1, 2, 16, 2.0)),
        "panel_scales": jnp.clip(jnp.exp(math.log(0.01711633) - 2.3025852 * jax.random.uniform(key_list[3], (NQ, V, NBLK), jnp.float32) ** levels(key_list[3], (NQ, V, NBLK), ((0, 16), (1, 16)), -0.2, 0.2)), 0.0017116329, 0.01711633),
        "amplitudes": scatter_about(key_list[4], (NPAIRS, V, V), V ** -0.5, 0.125, ((0, 16), (1, 16))),
    }


def reference(row_codes, row_scales, panel_codes, panel_scales, amplitudes):
    row_decoded = (row_codes.astype(jnp.float32).reshape(NQ, AW, NBLK, BLK) * row_scales[:, :, :, None]).reshape(NQ, AW, V).astype(jnp.bfloat16)
    panel_decoded = (panel_codes.astype(jnp.float32).reshape(NQ, V, NBLK, BLK) * panel_scales[:, :, :, None]).reshape(NQ, V, V).astype(jnp.bfloat16)
    row_wide = row_decoded.astype(jnp.float32)
    panel_wide = panel_decoded.astype(jnp.float32)

    def one_pair(amp):
        half = jnp.einsum("qac,dc->qda", row_wide, amp.astype(jnp.float32)).astype(jnp.bfloat16)
        return jnp.einsum("qdb,qda->ba", panel_wide, half.astype(jnp.float32))

    result = lax.map(one_pair, amplitudes)
    return jnp.transpose(result, (1, 0, 2))
```

```python
import jax
import jax.numpy as jnp
from jax import lax
from jax.sharding import PartitionSpec as P


def decode_rows(codes, scales):
    count, width, length = codes.shape
    blocks = scales.shape[2]
    wide = (
        codes.astype(jnp.float32).reshape(count, width, blocks, length // blocks)
        * scales[:, :, :, None]
    )
    return wide.reshape(count, width, length).astype(jnp.bfloat16)


def on_device(row_codes, row_scales, panel_codes, panel_scales, amplitudes):
    row_local = decode_rows(row_codes, row_scales)
    panel_local = decode_rows(panel_codes, panel_scales)
    row_all = lax.all_gather(row_local, "aux", axis=0, tiled=True)
    half = jnp.einsum(
        "qac,pdc->pqda", row_all, amplitudes, preferred_element_type=jnp.float32
    ).astype(jnp.bfloat16)
    total = jnp.einsum(
        "qdb,pqda->bpa",
        lax.all_gather(panel_local, "aux", axis=0, tiled=True),
        half,
        preferred_element_type=jnp.float32,
    )
    parts = lax.axis_size("virt")
    width = total.shape[0] // parts
    sent = total.astype(jnp.bfloat16).reshape(parts, width, *total.shape[1:])
    got = lax.all_to_all(sent, "virt", 0, 0, tiled=True)
    return got.astype(jnp.float32).sum(axis=0)


def solution(mesh):
    placed = (
        P("aux", None, None),
        P("aux", None, None),
        P("aux", "virt", None),
        P("aux", "virt", None),
        P("aux", "virt", None),
    )
    return jax.shard_map(
        on_device, mesh=mesh, in_specs=placed, out_specs=P("virt", "aux", None), check_vma=False
    )
```

```python
import jax
import jax.numpy as jnp
from jax import lax
from jax.sharding import PartitionSpec as P


def decode_rows(codes, scales):
    count, width, length = codes.shape
    blocks = scales.shape[2]
    wide = (
        codes.astype(jnp.float32).reshape(count, width, blocks, length // blocks)
        * scales[:, :, :, None]
    )
    return wide.reshape(count, width, length).astype(jnp.bfloat16)


def on_device(row_codes, row_scales, panel_codes, panel_scales, amplitudes):
    row_local = decode_rows(row_codes, row_scales)
    panel_local = decode_rows(panel_codes, panel_scales)
    rows = row_local.shape[1]
    both = lax.all_gather(
        jnp.concatenate([row_local, panel_local], axis=1), "aux", axis=0, tiled=True
    )
    row_all = both[:, :rows]
    panel_all = both[:, rows:]
    half = jnp.einsum(
        "qac,pdc->pqda", row_all, amplitudes, preferred_element_type=jnp.float32
    ).astype(jnp.bfloat16)
    total = jnp.einsum(
        "qdb,pqda->bpa", panel_all, half, preferred_element_type=jnp.float32
    )
    parts = lax.axis_size("virt")
    width = total.shape[0] // parts
    sent = total.astype(jnp.bfloat16).reshape(parts, width, *total.shape[1:])
    got = lax.all_to_all(sent, "virt", 0, 0, tiled=True)
    return got.astype(jnp.float32).sum(axis=0)


def solution(mesh):
    placed = (
        P("aux", None, None),
        P("aux", None, None),
        P("aux", "virt", None),
        P("aux", "virt", None),
        P("aux", "virt", None),
    )
    return jax.shard_map(
        on_device, mesh=mesh, in_specs=placed, out_specs=P("virt", "aux", None), check_vma=False
    )
```

```python
import jax
import jax.numpy as jnp
from jax import lax
from jax.sharding import Mesh
from jax.sharding import PartitionSpec as P

AUX = ("z_hi", "y", "core")
VIRT = ("x", "z_lo")


def decode_rows(codes, scales):
    count, width, length = codes.shape
    blocks = scales.shape[2]
    wide = (
        codes.astype(jnp.float32).reshape(count, width, blocks, length // blocks)
        * scales[:, :, :, None]
    )
    return wide.reshape(count, width, length).astype(jnp.bfloat16)


def on_device(row_codes, row_scales, panel_codes, panel_scales, amplitudes):
    row_local = decode_rows(row_codes, row_scales)
    panel_local = decode_rows(panel_codes, panel_scales)
    rows = row_local.shape[1]
    mine = jnp.concatenate([row_local, panel_local], axis=1)
    halves = lax.axis_size("z_hi")
    other = lax.ppermute(mine, "z_hi", [(i, (i + 1) % halves) for i in range(halves)])
    both = lax.all_gather(
        jnp.stack([mine, other], axis=1), ("y", "core"), axis=0, tiled=True
    )
    row_all = both[:, :, :rows]
    panel_all = both[:, :, rows:]
    half = jnp.einsum(
        "gsac,pdc->pgsda", row_all, amplitudes, preferred_element_type=jnp.float32
    ).astype(jnp.bfloat16)
    total = jnp.einsum(
        "gsdb,pgsda->bpa", panel_all, half, preferred_element_type=jnp.float32
    )
    parts = lax.axis_size(VIRT)
    width = total.shape[0] // parts
    sent = total.astype(jnp.bfloat16).reshape(parts, width, *total.shape[1:])
    got = lax.all_to_all(sent, VIRT, 0, 0, tiled=True)
    return got.astype(jnp.float32).sum(axis=0)


def solution(mesh):
    sizes = dict(z_hi=2, y=4, core=2, x=4, z_lo=4)
    fine = Mesh(mesh.devices.reshape([sizes[n] for n in AUX + VIRT]), AUX + VIRT)
    placed = (
        P(AUX, None, None),
        P(AUX, None, None),
        P(AUX, VIRT, None),
        P(AUX, VIRT, None),
        P(AUX, VIRT, None),
    )
    return jax.shard_map(
        on_device, mesh=fine, in_specs=placed, out_specs=P(VIRT, AUX, None), check_vma=False
    )
```

```python
import jax
import jax.numpy as jnp
from jax import lax
from jax.sharding import Mesh
from jax.sharding import PartitionSpec as P

AUX = ("z_hi", "y", "core")
VIRT = ("x", "z_lo")


def decode_rows(codes, scales):
    count, width, length = codes.shape
    blocks = scales.shape[2]
    wide = (
        codes.astype(jnp.float32).reshape(count, width, blocks, length // blocks)
        * scales[:, :, :, None]
    )
    return wide.reshape(count, width, length).astype(jnp.bfloat16)


def on_device(row_codes, row_scales, panel_codes, panel_scales, amplitudes):
    row_local = decode_rows(row_codes, row_scales)
    panel_local = decode_rows(panel_codes, panel_scales)
    rows = row_local.shape[1]
    mine = jnp.concatenate([row_local, panel_local], axis=1)
    halves = lax.axis_size("z_hi")
    other = lax.ppermute(mine, "z_hi", [(i, (i + 1) % halves) for i in range(halves)])
    total = None
    for blocks in (mine, other):
        gathered = lax.all_gather(blocks, ("y", "core"), axis=0, tiled=True)
        half = jnp.einsum(
            "qac,pdc->pqda", gathered[:, :rows], amplitudes, preferred_element_type=jnp.float32
        ).astype(jnp.bfloat16)
        part = jnp.einsum(
            "qdb,pqda->bpa", gathered[:, rows:], half, preferred_element_type=jnp.float32
        )
        total = part if total is None else total + part
    parts = lax.axis_size(VIRT)
    width = total.shape[0] // parts
    sent = total.astype(jnp.bfloat16).reshape(parts, width, *total.shape[1:])
    got = lax.all_to_all(sent, VIRT, 0, 0, tiled=True)
    return got.astype(jnp.float32).sum(axis=0)


def solution(mesh):
    sizes = dict(z_hi=2, y=4, core=2, x=4, z_lo=4)
    fine = Mesh(mesh.devices.reshape([sizes[n] for n in AUX + VIRT]), AUX + VIRT)
    placed = (
        P(AUX, None, None),
        P(AUX, None, None),
        P(AUX, VIRT, None),
        P(AUX, VIRT, None),
        P(AUX, VIRT, None),
    )
    return jax.shard_map(
        on_device, mesh=fine, in_specs=placed, out_specs=P(VIRT, AUX, None), check_vma=False
    )
```

```python
import jax
import jax.numpy as jnp
from jax import lax
from jax.sharding import Mesh
from jax.sharding import PartitionSpec as P

AUX = ("z_hi", "y", "core")
VIRT = ("x", "z_lo")


def decode_rows(codes, scales):
    count, width, length = codes.shape
    blocks = scales.shape[2]
    wide = (
        codes.astype(jnp.float32).reshape(count, width, blocks, length // blocks)
        * scales[:, :, :, None]
    )
    return wide.reshape(count, width, length).astype(jnp.bfloat16)


def on_device(row_codes, row_scales, panel_codes, panel_scales, amplitudes):
    row_local = decode_rows(row_codes, row_scales)
    panel_local = decode_rows(panel_codes, panel_scales)
    rows = row_local.shape[1]
    mine = jnp.concatenate([row_local, panel_local], axis=1)
    halves = lax.axis_size("z_hi")
    other = lax.ppermute(mine, "z_hi", [(i, (i + 1) % halves) for i in range(halves)])
    total = None
    for blocks in (mine, other):
        gathered = lax.all_gather(blocks, ("y", "core"), axis=0, tiled=True)
        half = jnp.einsum(
            "qac,pdc->pqda", gathered[:, :rows], amplitudes, preferred_element_type=jnp.float32
        ).astype(jnp.bfloat16)
        part = jnp.einsum(
            "qdb,pqda->bpa", gathered[:, rows:], half, preferred_element_type=jnp.float32
        )
        total = part if total is None else total + part
    across, along = lax.axis_size("x"), lax.axis_size("z_lo")
    width = total.shape[0] // (across * along)
    sent = total.astype(jnp.bfloat16).reshape(across, along, width, *total.shape[1:])
    got = lax.all_to_all(sent, "x", 0, 0, tiled=True)
    summed = got.astype(jnp.float32).sum(axis=0).astype(jnp.bfloat16)
    got = lax.all_to_all(summed, "z_lo", 0, 0, tiled=True)
    return got.astype(jnp.float32).sum(axis=0)

def solution(mesh):
    sizes = dict(z_hi=2, y=4, core=2, x=4, z_lo=4)
    fine = Mesh(mesh.devices.reshape([sizes[n] for n in AUX + VIRT]), AUX + VIRT)
    placed = (
        P(AUX, None, None),
        P(AUX, None, None),
        P(AUX, VIRT, None),
        P(AUX, VIRT, None),
        P(AUX, VIRT, None),
    )
    return jax.shard_map(
        on_device, mesh=fine, in_specs=placed, out_specs=P(VIRT, AUX, None), check_vma=False
    )
```

```python
import jax
import jax.numpy as jnp
from jax import lax
from jax.sharding import Mesh
from jax.sharding import PartitionSpec as P

AUX = ("z_hi", "y", "core")
VIRT = ("x", "z_lo")


def decode_rows(codes, scales):
    count, width, length = codes.shape
    blocks = scales.shape[2]
    wide = (
        codes.astype(jnp.float32).reshape(count, width, blocks, length // blocks)
        * scales[:, :, :, None]
    )
    return wide.reshape(count, width, length).astype(jnp.bfloat16)


def gather_y_core(blocks):
    ring = lax.axis_size("y")
    up = [(i, (i + 1) % ring) for i in range(ring)]
    down = [(i, (i - 1) % ring) for i in range(ring)]
    from_below = lax.ppermute(blocks, "y", up)
    from_above = lax.ppermute(blocks, "y", down)
    cut = blocks.shape[2] // 2
    far = jnp.concatenate(
        [
            lax.ppermute(from_below[:, :, :cut], "y", up),
            lax.ppermute(from_above[:, :, cut:], "y", down),
        ],
        axis=2,
    )
    chip = jnp.concatenate([blocks, from_below, far, from_above], axis=0)
    other_core = lax.ppermute(chip, "core", [(0, 1), (1, 0)])
    return jnp.concatenate([chip, other_core], axis=0)


def on_device(row_codes, row_scales, panel_codes, panel_scales, amplitudes):
    row_local = decode_rows(row_codes, row_scales)
    panel_local = decode_rows(panel_codes, panel_scales)
    rows = row_local.shape[1]
    mine = jnp.concatenate([row_local, panel_local], axis=1)
    halves = lax.axis_size("z_hi")
    other = lax.ppermute(mine, "z_hi", [(i, (i + 1) % halves) for i in range(halves)])
    total = None
    for blocks in (mine, other):
        gathered = gather_y_core(blocks)
        half = jnp.einsum(
            "qac,pdc->pqda", gathered[:, :rows], amplitudes, preferred_element_type=jnp.float32
        ).astype(jnp.bfloat16)
        part = jnp.einsum(
            "qdb,pqda->bpa", gathered[:, rows:], half, preferred_element_type=jnp.float32
        )
        total = part if total is None else total + part
    across, along = lax.axis_size("x"), lax.axis_size("z_lo")
    width = total.shape[0] // (across * along)
    sent = total.astype(jnp.bfloat16).reshape(across, along, width, *total.shape[1:])
    got = lax.all_to_all(sent, "x", 0, 0, tiled=True)
    summed = got.astype(jnp.float32).sum(axis=0).astype(jnp.bfloat16)
    got = lax.all_to_all(summed, "z_lo", 0, 0, tiled=True)
    return got.astype(jnp.float32).sum(axis=0)

def solution(mesh):
    sizes = dict(z_hi=2, y=4, core=2, x=4, z_lo=4)
    fine = Mesh(mesh.devices.reshape([sizes[n] for n in AUX + VIRT]), AUX + VIRT)
    placed = (
        P(AUX, None, None),
        P(AUX, None, None),
        P(AUX, VIRT, None),
        P(AUX, VIRT, None),
        P(AUX, VIRT, None),
    )
    return jax.shard_map(
        on_device, mesh=fine, in_specs=placed, out_specs=P(VIRT, AUX, None), check_vma=False
    )
```

```python
import jax
import jax.numpy as jnp
from jax import lax
from jax.sharding import Mesh
from jax.sharding import PartitionSpec as P

AUX = ("z_hi", "y", "core")
VIRT = ("x", "z_lo")


def decode_rows(codes, scales):
    count, width, length = codes.shape
    blocks = scales.shape[2]
    wide = (
        codes.astype(jnp.float32).reshape(count, width, blocks, length // blocks)
        * scales[:, :, :, None]
    )
    return wide.reshape(count, width, length).astype(jnp.bfloat16)


def gather_y_core(blocks, after):
    ring = lax.axis_size("y")
    up = [(i, (i + 1) % ring) for i in range(ring)]
    down = [(i, (i - 1) % ring) for i in range(ring)]
    from_below = lax.ppermute(blocks, "y", up)
    from_above = lax.ppermute(blocks, "y", down)
    if after is not None:
        after, from_below, from_above = lax.optimization_barrier((after, from_below, from_above))
    cut = blocks.shape[2] // 2
    far = jnp.concatenate(
        [
            lax.ppermute(from_below[:, :, :cut], "y", up),
            lax.ppermute(from_above[:, :, cut:], "y", down),
        ],
        axis=2,
    )
    chip = jnp.concatenate([blocks, from_below, far, from_above], axis=0)
    other_core = lax.ppermute(chip, "core", [(0, 1), (1, 0)])
    return jnp.concatenate([chip, other_core], axis=0), after


def ladder(row_codes, row_scales, panel_codes, panel_scales, amplitudes):
    row_local = decode_rows(row_codes, row_scales)
    panel_local = decode_rows(panel_codes, panel_scales)
    rows = row_local.shape[1]
    mine = jnp.concatenate([row_local, panel_local], axis=1)
    halves = lax.axis_size("z_hi")
    other = lax.ppermute(mine, "z_hi", [(i, (i + 1) % halves) for i in range(halves)])
    total = None
    for blocks in (mine, other):
        gathered, total = gather_y_core(blocks, total)
        half = jnp.einsum(
            "qac,pdc->pqda", gathered[:, :rows], amplitudes, preferred_element_type=jnp.float32
        ).astype(jnp.bfloat16)
        part = jnp.einsum(
            "qdb,pqda->bpa", gathered[:, rows:], half, preferred_element_type=jnp.float32
        )
        total = part if total is None else total + part
    across, along = lax.axis_size("x"), lax.axis_size("z_lo")
    width = total.shape[0] // (across * along)
    sent = total.astype(jnp.bfloat16).reshape(across, along, width, *total.shape[1:])
    got = lax.all_to_all(sent, "x", 0, 0, tiled=True)
    summed = got.astype(jnp.float32).sum(axis=0).astype(jnp.bfloat16)
    got = lax.all_to_all(summed, "z_lo", 0, 0, tiled=True)
    return got.astype(jnp.float32).sum(axis=0)


def solution(mesh):
    sizes = dict(z_hi=2, y=4, core=2, x=4, z_lo=4)
    fine = Mesh(mesh.devices.reshape([sizes[n] for n in AUX + VIRT]), AUX + VIRT)
    placed = (
        P(AUX, None, None),
        P(AUX, None, None),
        P(AUX, VIRT, None),
        P(AUX, VIRT, None),
        P(AUX, VIRT, None),
    )
    return jax.shard_map(
        ladder, mesh=fine, in_specs=placed, out_specs=P(VIRT, AUX, None), check_vma=False
    )
```

```python
import jax
import jax.numpy as jnp
from jax import lax
from jax.sharding import Mesh
from jax.sharding import PartitionSpec as P

AUX = ("z_hi", "y", "core")
VIRT = ("x", "z_lo")


def decode_rows(codes, scales):
    count, width, length = codes.shape
    blocks = scales.shape[2]
    wide = (
        codes.astype(jnp.float32).reshape(count, width, blocks, length // blocks)
        * scales[:, :, :, None]
    )
    return wide.reshape(count, width, length).astype(jnp.bfloat16)


def gather_y_core(blocks, after):
    ring = lax.axis_size("y")
    up = [(i, (i + 1) % ring) for i in range(ring)]
    down = [(i, (i - 1) % ring) for i in range(ring)]
    from_below = lax.ppermute(blocks, "y", up)
    from_above = lax.ppermute(blocks, "y", down)
    if after is not None:
        after, from_below, from_above = lax.optimization_barrier((after, from_below, from_above))
    cut = blocks.shape[2] // 2
    far = jnp.concatenate(
        [
            lax.ppermute(from_below[:, :, :cut], "y", up),
            lax.ppermute(from_above[:, :, cut:], "y", down),
        ],
        axis=2,
    )
    chip = jnp.concatenate([blocks, from_below, far, from_above], axis=0)
    other_core = lax.ppermute(chip, "core", [(0, 1), (1, 0)])
    return (chip, other_core), after


def ladder(row_codes, row_scales, panel_codes, panel_scales, amplitudes):
    row_local = decode_rows(row_codes, row_scales)
    panel_local = decode_rows(panel_codes, panel_scales)
    rows = row_local.shape[1]
    mine = jnp.concatenate([row_local, panel_local], axis=1)
    halves = lax.axis_size("z_hi")
    other = lax.ppermute(mine, "z_hi", [(i, (i + 1) % halves) for i in range(halves)])
    total = None
    for blocks in (mine, other):
        pieces, total = gather_y_core(blocks, total)
        for gathered in pieces:
            half = jnp.einsum(
                "qac,pdc->pqda", gathered[:, :rows], amplitudes, preferred_element_type=jnp.float32
            ).astype(jnp.bfloat16)
            part = jnp.einsum(
                "qdb,pqda->bpa", gathered[:, rows:], half, preferred_element_type=jnp.float32
            )
            total = part if total is None else total + part
    across, along = lax.axis_size("x"), lax.axis_size("z_lo")
    width = total.shape[0] // (across * along)
    sent = total.astype(jnp.bfloat16).reshape(across, along, width, *total.shape[1:])
    got = lax.all_to_all(sent, "x", 0, 0, tiled=True)
    summed = got.astype(jnp.float32).sum(axis=0).astype(jnp.bfloat16)
    got = lax.all_to_all(summed, "z_lo", 0, 0, tiled=True)
    return got.astype(jnp.float32).sum(axis=0)


def solution(mesh):
    sizes = dict(z_hi=2, y=4, core=2, x=4, z_lo=4)
    fine = Mesh(mesh.devices.reshape([sizes[n] for n in AUX + VIRT]), AUX + VIRT)
    placed = (
        P(AUX, None, None),
        P(AUX, None, None),
        P(AUX, VIRT, None),
        P(AUX, VIRT, None),
        P(AUX, VIRT, None),
    )
    return jax.shard_map(
        ladder, mesh=fine, in_specs=placed, out_specs=P(VIRT, AUX, None), check_vma=False
    )
```

```python
import jax
import jax.numpy as jnp
from jax import lax
from jax.sharding import Mesh
from jax.sharding import PartitionSpec as P

AUX = ("z_hi", "y", "core")
VIRT = ("x", "z_lo")


def decode_rows(codes, scales):
    count, width, length = codes.shape
    blocks = scales.shape[2]
    wide = (
        codes.astype(jnp.float32).reshape(count, width, blocks, length // blocks)
        * scales[:, :, :, None]
    )
    return wide.reshape(count, width, length).astype(jnp.bfloat16)


def gather_y_core(blocks, after):
    ring = lax.axis_size("y")
    up = [(i, (i + 1) % ring) for i in range(ring)]
    down = [(i, (i - 1) % ring) for i in range(ring)]
    from_below = lax.ppermute(blocks, "y", up)
    from_above = lax.ppermute(blocks, "y", down)
    if after is not None:
        after, from_below, from_above = lax.optimization_barrier((after, from_below, from_above))
    cut = blocks.shape[2] // 2
    far = jnp.concatenate(
        [
            lax.ppermute(from_below[:, :, :cut], "y", up),
            lax.ppermute(from_above[:, :, cut:], "y", down),
        ],
        axis=2,
    )
    chip = jnp.concatenate([blocks, from_below, far, from_above], axis=0)
    other_core = lax.ppermute(chip, "core", [(0, 1), (1, 0)])
    return (chip, other_core), after


def ladder(row_codes, row_scales, panel_codes, panel_scales, amplitudes):
    row_local = decode_rows(row_codes, row_scales)
    panel_local = decode_rows(panel_codes, panel_scales)
    rows = row_local.shape[1]
    mine = jnp.concatenate([row_local, panel_local], axis=1)
    halves = lax.axis_size("z_hi")
    other = lax.ppermute(mine, "z_hi", [(i, (i + 1) % halves) for i in range(halves)])
    total = None
    for blocks in (mine, other):
        pieces, total = gather_y_core(blocks, total)
        halves_of = [
            jnp.einsum(
                "qac,pdc->pqda", gathered[:, :rows], amplitudes, preferred_element_type=jnp.float32
            ).astype(jnp.bfloat16)
            for gathered in pieces
        ]
        part = jnp.einsum(
            "qdb,pqda->bpa",
            jnp.concatenate([gathered[:, rows:] for gathered in pieces], axis=0),
            jnp.concatenate(halves_of, axis=1),
            preferred_element_type=jnp.float32,
        )
        total = part if total is None else total + part
    across, along = lax.axis_size("x"), lax.axis_size("z_lo")
    width = total.shape[0] // (across * along)
    sent = total.astype(jnp.bfloat16).reshape(across, along, width, *total.shape[1:])
    got = lax.all_to_all(sent, "x", 0, 0, tiled=True)
    summed = got.astype(jnp.float32).sum(axis=0).astype(jnp.bfloat16)
    got = lax.all_to_all(summed, "z_lo", 0, 0, tiled=True)
    return got.astype(jnp.float32).sum(axis=0)


def solution(mesh):
    sizes = dict(z_hi=2, y=4, core=2, x=4, z_lo=4)
    fine = Mesh(mesh.devices.reshape([sizes[n] for n in AUX + VIRT]), AUX + VIRT)
    placed = (
        P(AUX, None, None),
        P(AUX, None, None),
        P(AUX, VIRT, None),
        P(AUX, VIRT, None),
        P(AUX, VIRT, None),
    )
    return jax.shard_map(
        ladder, mesh=fine, in_specs=placed, out_specs=P(VIRT, AUX, None), check_vma=False
    )
```
